32 devices in a mesh: groups: 2 (over y), tok: 4 (over z), span: 2 (over x), head: 2 (over core).
Axes of the slice: x: 2, y: 2, z: 4, core: 2. Of those that a mesh axis runs over, the one named last changes fastest.
Arguments:
- key_rows: bfloat16 [6, 2, 2048, 2, 256], P('groups', 'span', 'tok', 'head'), parts along dimension 0, may hold values from -6 to 6
- value_rows: bfloat16 [6, 2, 2048, 2, 256], P('groups', 'span', 'tok', 'head'), parts along dimension 0, may hold values from -6 to 6
- query_rows: bfloat16 [6, 2, 2048, 2, 256], P('groups', 'span', 'tok', 'head'), parts along dimension 0, may hold values from -6 to 6
- step_rates: float32 [6, 2, 2, 2048], P('groups', 'span', 'head', 'tok'), parts along dimension 0, may hold values from 0.4 to 3
- states_in: float32 [4, 2, 3, 256, 256], P(('groups', 'span'), 'head', None, None, 'tok'), parts along dimension 0, may hold values from -0.375 to 0.375
- init_weights: bfloat16 [2, 3, 256, 256], P('head'), may hold values from -0.375 to 0.375
Outputs:
- outputs: bfloat16 [6, 2, 2048, 2, 256], P('groups', 'span', 'tok', 'head'), parts along dimension 0
- states_out: float32 [4, 2, 3, 256, 256], P(('groups', 'span'), 'head', None, None, 'tok'), parts along dimension 0
The draws below stay inside these ranges and needn't reach their ends.
There are 2 independent parts, one for each index of `groups`. The reference program is written for one: setup_inputs(seed, part) draws one part's arguments, and reference() takes and returns one part's arrays. A program takes and returns all parts, laid end to end along the dimension named above; an argument that names none is the same for every part. Nothing has to cross between parts.
All inputs are finite; a program needn't handle non-finite values.
Results may differ from the reference program's by a relative error of at most 0.039.
Values may be sent and summed in bfloat16 or wider, within the bound.
No kernel may reach another device: no remote copies, remote signals or barrier semaphores. Data moves between devices by JAX's collectives and lax.ppermute only.
A program may use at most 64 MiB of HBM per device.

```python
import math
import jax
import jax.numpy as jnp
from jax import lax

D = 256
TOK_DEV = 512
ITERS = 2
TICKS = 3
HEADS = 2
SPAN_LEN = 2048
SECTIONS = 2
N_TOK = 4


def level_of(own_key, shape, cuts, least, largest):
    factor_of, own = 1.0, jax.random.fold_in(own_key, 6)
    for axis_at, parts in cuts:
        heights = jnp.exp(jax.random.uniform(jax.random.fold_in(own, axis_at), (parts,), jnp.float32, least / len(cuts), largest / len(cuts)))
        factor_of = factor_of * jnp.repeat(heights, shape[axis_at] // parts).reshape([-1 if axis == axis_at else 1 for axis in range(len(shape))])
    return factor_of


def centred(stream_key, extent, deviation, bound, split=(), held_as=jnp.bfloat16):
    values = deviation * jax.random.normal(stream_key, extent, jnp.float32)
    if split:
        values = values * level_of(stream_key, extent, split, -0.22, 0.18)
    return jnp.clip(values, -bound, bound).astype(held_as)


def setup_inputs(seed: int = 0, part: int = 0) -> dict:
    arg_keys = jax.random.split(jax.random.key(seed), 7)
    part_keys = jax.random.split(jax.random.fold_in(arg_keys[6], part), 7)
    return {
        "key_rows": centred(part_keys[0], (TICKS, SECTIONS, SPAN_LEN, HEADS, D), 1.0, 6.0, ((1, 2), (2, 4), (3, 2))),
        "value_rows": centred(part_keys[1], (TICKS, SECTIONS, SPAN_LEN, HEADS, D), 1.0, 6.0, ((1, 2), (2, 4), (3, 2))),
        "query_rows": centred(part_keys[2], (TICKS, SECTIONS, SPAN_LEN, HEADS, D), 1.0, 6.0, ((1, 2), (2, 4), (3, 2))),
        "step_rates": jnp.clip(jnp.exp(math.log(3.0) - 2.014903 * jax.random.uniform(part_keys[3], (TICKS, SECTIONS, HEADS, SPAN_LEN), jnp.float32) ** level_of(part_keys[3], (TICKS, SECTIONS, HEADS, SPAN_LEN), ((1, 2), (2, 2), (3, 4)), -0.2, 0.2)), 0.4, 3.0),
        "states_in": centred(part_keys[4], (SECTIONS, HEADS, 3, D, D), D ** -0.5, 0.375, ((0, 2), (1, 2), (4, 4)), jnp.float32),
        "init_weights": centred(arg_keys[5], (HEADS, 3, D, D), D ** -0.5, 0.375, ((0, 2),)),
    }


def rounded(value):
    return lax.optimization_barrier(value.astype(jnp.bfloat16)).astype(jnp.float32)

def product(form, left, right):
    return jnp.einsum(form, left, right, precision=lax.Precision.HIGHEST)

def renormalize(matrices, init_norms):
    column_norms = jnp.sqrt(lax.optimization_barrier(jnp.sum(matrices * matrices, axis=-2)) + 1e-06)
    return matrices * (init_norms / column_norms)[..., None, :]

def process(weights, key_block, value_block, query_block, rate_block, init_norms):
    key_float = key_block.astype(jnp.float32)
    query_float = query_block.astype(jnp.float32)
    rate_scale = 1.0 / math.sqrt(SPAN_LEN * D)
    scaled = rounded((rate_block * rate_scale)[..., None] * value_block.astype(jnp.float32))
    for update_step in range(ITERS):
        fast = rounded(weights)
        gate_pre = product('ntd,dh->nth', key_float, fast[0])
        up_pre = product('ntd,dh->nth', key_float, fast[1])
        sigmoid_gate = jax.nn.sigmoid(gate_pre)
        gated = gate_pre * sigmoid_gate
        hidden = rounded(gated * up_pre)
        back_grad = product('ntd,hd->nth', scaled, fast[2])
        grad_gate = rounded(back_grad * up_pre * sigmoid_gate * (1.0 + gate_pre * (1.0 - sigmoid_gate)))
        grad_up = rounded(back_grad * gated)
        partial_value = jnp.stack([product('ntd,nth->ndh', key_float, grad_gate), product('ntd,nth->ndh', key_float, grad_up), product('nth,ntd->nhd', hidden, scaled)], axis=1)
        summed = lax.optimization_barrier(jnp.sum(rounded(partial_value), axis=0))
        weights = renormalize(weights + summed, init_norms)
    fast = rounded(weights)
    query_gate = product('ntd,dh->nth', query_float, fast[0])
    query_up = product('ntd,dh->nth', query_float, fast[1])
    applied = rounded(query_gate * jax.nn.sigmoid(query_gate) * query_up)
    result = product('nth,hd->ntd', applied, fast[2]).astype(jnp.bfloat16)
    return (weights, result)

def arrange(block):
    return block.reshape(SECTIONS, N_TOK, TOK_DEV, HEADS, D).transpose(0, 3, 1, 2, 4)

def reference(key_rows, value_rows, query_rows, step_rates, states_in, init_weights):
    init_full = init_weights.astype(jnp.float32)
    init_norms = jnp.sqrt(lax.optimization_barrier(jnp.sum(init_full * init_full, axis=-2)) + 1e-06)
    weights = states_in
    inner = jax.vmap(process, in_axes=(0, 0, 0, 0, 0, 0))
    outer = jax.vmap(inner, in_axes=(0, 0, 0, 0, 0, None))
    results = []
    for tick_number in range(TICKS):
        if tick_number > 0:
            weights = jnp.concatenate([init_full[None], weights[:-1]], axis=0)
        rate_block = step_rates[tick_number].reshape(SECTIONS, HEADS, N_TOK, TOK_DEV)
        weights, result = outer(weights, arrange(key_rows[tick_number]), arrange(value_rows[tick_number]), arrange(query_rows[tick_number]), rate_block, init_norms)
        results.append(result.transpose(0, 2, 3, 1, 4).reshape(SECTIONS, SPAN_LEN, HEADS, D))
    return (jnp.stack(results), weights)
```

```python
import math

import jax
import jax.numpy as jnp
from jax import lax
from jax.sharding import PartitionSpec as P

ITERS = 2


def shifted(value, axis, by):
    devices = lax.axis_size(axis)
    pairs = [(i, i + by) for i in range(devices) if 0 <= i + by < devices]
    return lax.ppermute(value, axis, pairs)


def rotated(value, axis, by):
    devices = lax.axis_size(axis)
    return lax.ppermute(value, axis, [(i, (i + by) % devices) for i in range(devices)])


def scatter_sum(partial, part_cols):
    tok_count = lax.axis_size("tok")
    me = lax.axis_index("tok")
    total = lax.dynamic_slice_in_dim(partial, me * part_cols, part_cols, 2).astype(jnp.float32)
    for by in range(1, tok_count):
        chunk = lax.dynamic_slice_in_dim(partial, ((me + by) % tok_count) * part_cols, part_cols, 2)
        total = total + rotated(chunk, "tok", by).astype(jnp.float32)
    return total


def gather_cols(own, part_cols):
    tok_count = lax.axis_size("tok")
    me = lax.axis_index("tok")
    full = jnp.zeros(own.shape[:2] + (part_cols * tok_count,), own.dtype)
    full = lax.dynamic_update_slice_in_dim(full, own, me * part_cols, 2)
    for by in range(1, tok_count):
        got = rotated(own, "tok", by)
        full = lax.dynamic_update_slice_in_dim(full, got, ((me - by) % tok_count) * part_cols, 2)
    return full


def renormalize(matrices, init_norms):
    column_norms = jnp.sqrt(jnp.sum(matrices * matrices, axis=-2) + 1e-06)
    return matrices * (init_norms / column_norms)[..., None, :]


def fast_grads(fast, key_block, scaled):
    gate_pre = jnp.einsum("td,dh->th", key_block, fast[0], preferred_element_type=jnp.float32)
    up_pre = jnp.einsum("td,dh->th", key_block, fast[1], preferred_element_type=jnp.float32)
    sigmoid_gate = jax.nn.sigmoid(gate_pre)
    gated = gate_pre * sigmoid_gate
    hidden = (gated * up_pre).astype(jnp.bfloat16)
    back_grad = jnp.einsum("td,hd->th", scaled, fast[2], preferred_element_type=jnp.float32)
    grad_gate = (
        back_grad * up_pre * sigmoid_gate * (1.0 + gate_pre * (1.0 - sigmoid_gate))
    ).astype(jnp.bfloat16)
    grad_up = (back_grad * gated).astype(jnp.bfloat16)
    first = jnp.einsum("td,th->dh", key_block, grad_gate, preferred_element_type=jnp.float32)
    second = jnp.einsum("td,th->dh", key_block, grad_up, preferred_element_type=jnp.float32)
    third = jnp.einsum("th,td->hd", hidden, scaled, preferred_element_type=jnp.float32)
    return jnp.stack([first, second, third], axis=0).astype(jnp.bfloat16)


def apply_fast(fast, query_block):
    query_gate = jnp.einsum("td,dh->th", query_block, fast[0], preferred_element_type=jnp.float32)
    query_up = jnp.einsum("td,dh->th", query_block, fast[1], preferred_element_type=jnp.float32)
    applied = (query_gate * jax.nn.sigmoid(query_gate) * query_up).astype(jnp.bfloat16)
    return jnp.einsum(
        "th,hd->td", applied, fast[2], preferred_element_type=jnp.float32
    ).astype(jnp.bfloat16)


def on_device(key_rows, value_rows, query_rows, step_rates, states_in, init_weights):
    tok_count = lax.axis_size("tok")
    feature_width = init_weights.shape[-1]
    part_cols = feature_width // tok_count
    rate_scale = 1.0 / math.sqrt(key_rows.shape[2] * tok_count * feature_width)
    section_index = lax.axis_index("span")
    tok_index = lax.axis_index("tok")
    init_fast = init_weights[0]
    init_full = init_fast.astype(jnp.float32)
    init_norms = jnp.sqrt(jnp.sum(init_full * init_full, axis=-2) + 1e-06)
    own_norms = lax.dynamic_slice_in_dim(init_norms, tok_index * part_cols, part_cols, 1)
    tick_count = key_rows.shape[0]
    results = []
    weights = states_in[0, 0]
    fast = gather_cols(weights.astype(jnp.bfloat16), part_cols)
    for tick_number in range(tick_count):
        if tick_number > 0:
            arrived = shifted(fast, "span", 1)
            fast = jnp.where(section_index == 0, init_fast, arrived)
            weights = lax.dynamic_slice_in_dim(fast, tok_index * part_cols, part_cols, 2).astype(
                jnp.float32
            )
        key_block = key_rows[tick_number, 0, :, 0]
        scaled = (
            (step_rates[tick_number, 0, 0] * rate_scale)[:, None]
            * value_rows[tick_number, 0, :, 0].astype(jnp.float32)
        ).astype(jnp.bfloat16)
        for update_step in range(ITERS):
            if update_step > 0:
                fast = gather_cols(weights.astype(jnp.bfloat16), part_cols)
            summed = scatter_sum(fast_grads(fast, key_block, scaled), part_cols)
            weights = renormalize(weights + summed, own_norms)
        fast = gather_cols(weights.astype(jnp.bfloat16), part_cols)
        results.append(apply_fast(fast, query_rows[tick_number, 0, :, 0]))
    outputs = jnp.stack(results)[:, None, :, None]
    return (outputs, weights[None, None])


def solution(mesh):
    placed = (
        P("groups", "span", "tok", "head", None),
        P("groups", "span", "tok", "head", None),
        P("groups", "span", "tok", "head", None),
        P("groups", "span", "head", "tok"),
        P(("groups", "span"), "head", None, None, "tok"),
        P("head", None, None, None),
    )
    return jax.shard_map(
        on_device,
        mesh=mesh,
        in_specs=placed,
        out_specs=(
            P("groups", "span", "tok", "head", None),
            P(("groups", "span"), "head", None, None, "tok"),
        ),
        check_vma=False,
    )
```

```python
import math

import jax
import jax.numpy as jnp
from jax import lax
from jax.sharding import PartitionSpec as P

ITERS = 2


def shifted(value, axis, by):
    devices = lax.axis_size(axis)
    pairs = [(i, i + by) for i in range(devices) if 0 <= i + by < devices]
    return lax.ppermute(value, axis, pairs)


def rotated(value, axis, by):
    devices = lax.axis_size(axis)
    return lax.ppermute(value, axis, [(i, (i + by) % devices) for i in range(devices)])


def gathered(value):
    tok_count = lax.axis_size("tok")
    return jnp.stack([value] + [rotated(value, "tok", by) for by in range(1, tok_count)])


def summed_over_tok(value):
    tok_count = lax.axis_size("tok")
    total = value
    for by in range(1, tok_count):
        total = total + rotated(value, "tok", by)
    return total


def to_rows(cols):
    tok_count = lax.axis_size("tok")
    part = cols.shape[1]
    pieces = cols.reshape(tok_count, part, part)
    got = lax.all_to_all(pieces, "tok", 0, 0, tiled=False)
    return jnp.transpose(got, (0, 2, 1)).reshape(tok_count * part, part)


def to_cols(rows_t):
    tok_count = lax.axis_size("tok")
    part = rows_t.shape[1]
    pieces = jnp.transpose(rows_t.reshape(tok_count, part, part), (0, 2, 1))
    got = lax.all_to_all(pieces, "tok", 0, 0, tiled=False)
    return got.reshape(tok_count * part, part)


def update(weights, keys, scaled, own_norms):
    fast = weights.astype(jnp.bfloat16)
    gate_pre = jnp.einsum("btd,dh->bth", keys, fast[0], preferred_element_type=jnp.float32)
    up_pre = jnp.einsum("btd,dh->bth", keys, fast[1], preferred_element_type=jnp.float32)
    back_grad = jnp.einsum("btd,dh->bth", scaled, fast[2], preferred_element_type=jnp.float32)
    sigmoid_gate = jax.nn.sigmoid(gate_pre)
    gated = gate_pre * sigmoid_gate
    hidden = (gated * up_pre).astype(jnp.bfloat16)
    grad_gate = (
        back_grad * up_pre * sigmoid_gate * (1.0 + gate_pre * (1.0 - sigmoid_gate))
    ).astype(jnp.bfloat16)
    grad_up = (back_grad * gated).astype(jnp.bfloat16)
    first = jnp.einsum("btd,bth->bdh", keys, grad_gate, preferred_element_type=jnp.float32)
    second = jnp.einsum("btd,bth->bdh", keys, grad_up, preferred_element_type=jnp.float32)
    third = jnp.einsum("btd,bth->bdh", scaled, hidden, preferred_element_type=jnp.float32)
    partial = jnp.stack([first, second, third], axis=1).astype(jnp.bfloat16)
    weights = weights + jnp.sum(partial.astype(jnp.float32), axis=0)
    squares = jnp.sum(weights * weights, axis=1)
    first_two = jnp.sqrt(squares[:2] + 1e-06)
    w2_squares = summed_over_tok(jnp.sum(weights[2] * weights[2], axis=1))
    w2_norms = jnp.sqrt(w2_squares + 1e-06)
    top = weights[:2] * (own_norms[0] / first_two)[:, None, :]
    last = weights[2] * (own_norms[1] / w2_norms)[:, None]
    return jnp.concatenate([top, last[None]], axis=0)


def apply_fast(weights, query_block):
    fast = jnp.concatenate(gathered(weights.astype(jnp.bfloat16)), axis=-1)
    query_gate = jnp.einsum("td,dh->th", query_block, fast[0], preferred_element_type=jnp.float32)
    query_up = jnp.einsum("td,dh->th", query_block, fast[1], preferred_element_type=jnp.float32)
    applied = (query_gate * jax.nn.sigmoid(query_gate) * query_up).astype(jnp.bfloat16)
    return jnp.einsum(
        "th,dh->td", applied, fast[2], preferred_element_type=jnp.float32
    ).astype(jnp.bfloat16)


def on_device(key_rows, value_rows, query_rows, step_rates, states_in, init_weights):
    tok_count = lax.axis_size("tok")
    feature_width = init_weights.shape[-1]
    part = feature_width // tok_count
    rate_scale = 1.0 / math.sqrt(key_rows.shape[2] * tok_count * feature_width)
    section_index = lax.axis_index("span")
    tok_index = lax.axis_index("tok")
    init_full = init_weights[0].astype(jnp.float32)
    init_norms = jnp.sqrt(jnp.sum(init_full * init_full, axis=-2) + 1e-06)
    own_hidden = lambda m: lax.dynamic_slice_in_dim(m, tok_index * part, part, m.ndim - 1)
    own_norms = (jnp.stack([own_hidden(init_norms[0]), own_hidden(init_norms[1])]), init_norms[2])
    init_own = jnp.stack(
        [own_hidden(init_full[0]), own_hidden(init_full[1]), own_hidden(init_full[2].T)]
    )
    tick_count = key_rows.shape[0]
    blocks = []
    for tick_number in range(tick_count):
        scaled = (
            (step_rates[tick_number, 0, 0] * rate_scale)[:, None]
            * value_rows[tick_number, 0, :, 0].astype(jnp.float32)
        ).astype(jnp.bfloat16)
        blocks.append(gathered(jnp.stack([key_rows[tick_number, 0, :, 0], scaled])))
    start = states_in[0, 0]
    weights = jnp.stack([start[0], start[1], to_rows(start[2])])
    results = []
    for tick_number in range(tick_count):
        if tick_number > 0:
            arrived = shifted(weights, "span", 1)
            weights = jnp.where(section_index == 0, init_own, arrived)
        keys, scaled = blocks[tick_number][:, 0], blocks[tick_number][:, 1]
        for update_step in range(ITERS):
            weights = update(weights, keys, scaled, own_norms)
        results.append(apply_fast(weights, query_rows[tick_number, 0, :, 0]))
    outputs = jnp.stack(results)[:, None, :, None]
    final = jnp.stack([weights[0], weights[1], to_cols(weights[2])])
    return (outputs, final[None, None])


def solution(mesh):
    placed = (
        P("groups", "span", "tok", "head", None),
        P("groups", "span", "tok", "head", None),
        P("groups", "span", "tok", "head", None),
        P("groups", "span", "head", "tok"),
        P(("groups", "span"), "head", None, None, "tok"),
        P("head", None, None, None),
    )
    return jax.shard_map(
        on_device,
        mesh=mesh,
        in_specs=placed,
        out_specs=(
            P("groups", "span", "tok", "head", None),
            P(("groups", "span"), "head", None, None, "tok"),
        ),
        check_vma=False,
    )
```

```python
import math

import jax
import jax.numpy as jnp
from jax import lax
from jax.sharding import PartitionSpec as P

ITERS = 2


def shifted(value, axis, by):
    devices = lax.axis_size(axis)
    pairs = [(i, i + by) for i in range(devices) if 0 <= i + by < devices]
    return lax.ppermute(value, axis, pairs)


def rotated(value, axis, by):
    devices = lax.axis_size(axis)
    return lax.ppermute(value, axis, [(i, (i + by) % devices) for i in range(devices)])


def _halving_bits(tok_count):
    bits = tok_count.bit_length() - 1
    return bits if (1 << bits) == tok_count else None


def scatter_sum(partial, part_cols):
    tok_count = lax.axis_size("tok")
    me = lax.axis_index("tok")
    bits = _halving_bits(tok_count)
    if bits is None:
        total = lax.dynamic_slice_in_dim(partial, me * part_cols, part_cols, 2).astype(jnp.float32)
        for by in range(1, tok_count):
            chunk = lax.dynamic_slice_in_dim(partial, ((me + by) % tok_count) * part_cols, part_cols, 2)
            total = total + rotated(chunk, "tok", by).astype(jnp.float32)
        return total
    held = partial.reshape(partial.shape[:2] + (2,) * bits + (part_cols,))
    for bit in range(bits):
        axis = 2 + (bits - 1 - bit)
        mine = (me >> bit) & 1
        keep = lax.dynamic_index_in_dim(held, mine, axis, keepdims=False)
        send = lax.dynamic_index_in_dim(held, 1 - mine, axis, keepdims=False)
        got = lax.ppermute(
            send.astype(jnp.bfloat16), "tok", [(i, i ^ (1 << bit)) for i in range(tok_count)]
        )
        held = keep.astype(jnp.float32) + got.astype(jnp.float32)
    return held


def gather_cols(own, part_cols):
    tok_count = lax.axis_size("tok")
    me = lax.axis_index("tok")
    bits = _halving_bits(tok_count)
    if bits is None:
        full = jnp.zeros(own.shape[:2] + (part_cols * tok_count,), own.dtype)
        full = lax.dynamic_update_slice_in_dim(full, own, me * part_cols, 2)
        for by in range(1, tok_count):
            got = rotated(own, "tok", by)
            full = lax.dynamic_update_slice_in_dim(full, got, ((me - by) % tok_count) * part_cols, 2)
        return full
    held = own
    for bit in reversed(range(bits)):
        mine = (me >> bit) & 1
        got = lax.ppermute(held, "tok", [(i, i ^ (1 << bit)) for i in range(tok_count)])
        low = jnp.where(mine == 0, held, got)
        high = jnp.where(mine == 0, got, held)
        held = jnp.stack([low, high], axis=-2)
    return held.reshape(own.shape[:2] + (part_cols * tok_count,))


def renormalize(matrices, init_norms):
    column_norms = jnp.sqrt(jnp.sum(matrices * matrices, axis=-2) + 1e-06)
    return matrices * (init_norms / column_norms)[..., None, :]


def fast_grads(fast, key_block, scaled):
    gate_pre = jnp.einsum("td,dh->th", key_block, fast[0], preferred_element_type=jnp.float32)
    up_pre = jnp.einsum("td,dh->th", key_block, fast[1], preferred_element_type=jnp.float32)
    sigmoid_gate = jax.nn.sigmoid(gate_pre)
    gated = gate_pre * sigmoid_gate
    hidden = (gated * up_pre).astype(jnp.bfloat16)
    back_grad = jnp.einsum("td,hd->th", scaled, fast[2], preferred_element_type=jnp.float32)
    grad_gate = (
        back_grad * up_pre * sigmoid_gate * (1.0 + gate_pre * (1.0 - sigmoid_gate))
    ).astype(jnp.bfloat16)
    grad_up = (back_grad * gated).astype(jnp.bfloat16)
    first = jnp.einsum("td,th->dh", key_block, grad_gate, preferred_element_type=jnp.float32)
    second = jnp.einsum("td,th->dh", key_block, grad_up, preferred_element_type=jnp.float32)
    third = jnp.einsum("th,td->hd", hidden, scaled, preferred_element_type=jnp.float32)
    return jnp.stack([first, second, third], axis=0).astype(jnp.bfloat16)


def apply_fast(fast, query_block):
    query_gate = jnp.einsum("td,dh->th", query_block, fast[0], preferred_element_type=jnp.float32)
    query_up = jnp.einsum("td,dh->th", query_block, fast[1], preferred_element_type=jnp.float32)
    applied = (query_gate * jax.nn.sigmoid(query_gate) * query_up).astype(jnp.bfloat16)
    return jnp.einsum(
        "th,hd->td", applied, fast[2], preferred_element_type=jnp.float32
    ).astype(jnp.bfloat16)


def on_device(key_rows, value_rows, query_rows, step_rates, states_in, init_weights):
    tok_count = lax.axis_size("tok")
    feature_width = init_weights.shape[-1]
    part_cols = feature_width // tok_count
    rate_scale = 1.0 / math.sqrt(key_rows.shape[2] * tok_count * feature_width)
    section_index = lax.axis_index("span")
    tok_index = lax.axis_index("tok")
    init_fast = init_weights[0]
    init_full = init_fast.astype(jnp.float32)
    init_norms = jnp.sqrt(jnp.sum(init_full * init_full, axis=-2) + 1e-06)
    own_norms = lax.dynamic_slice_in_dim(init_norms, tok_index * part_cols, part_cols, 1)
    tick_count = key_rows.shape[0]
    results = []
    weights = states_in[0, 0]
    fast = gather_cols(weights.astype(jnp.bfloat16), part_cols)
    for tick_number in range(tick_count):
        if tick_number > 0:
            arrived = shifted(fast, "span", 1)
            fast = jnp.where(section_index == 0, init_fast, arrived)
            weights = lax.dynamic_slice_in_dim(fast, tok_index * part_cols, part_cols, 2).astype(
                jnp.float32
            )
        key_block = key_rows[tick_number, 0, :, 0]
        scaled = (
            (step_rates[tick_number, 0, 0] * rate_scale)[:, None]
            * value_rows[tick_number, 0, :, 0].astype(jnp.float32)
        ).astype(jnp.bfloat16)
        for update_step in range(ITERS):
            if update_step > 0:
                fast = gather_cols(weights.astype(jnp.bfloat16), part_cols)
            summed = scatter_sum(fast_grads(fast, key_block, scaled), part_cols)
            weights = renormalize(weights + summed, own_norms)
        fast = gather_cols(weights.astype(jnp.bfloat16), part_cols)
        results.append(apply_fast(fast, query_rows[tick_number, 0, :, 0]))
    outputs = jnp.stack(results)[:, None, :, None]
    return (outputs, weights[None, None])


def solution(mesh):
    placed = (
        P("groups", "span", "tok", "head", None),
        P("groups", "span", "tok", "head", None),
        P("groups", "span", "tok", "head", None),
        P("groups", "span", "head", "tok"),
        P(("groups", "span"), "head", None, None, "tok"),
        P("head", None, None, None),
    )
    return jax.shard_map(
        on_device,
        mesh=mesh,
        in_specs=placed,
        out_specs=(
            P("groups", "span", "tok", "head", None),
            P(("groups", "span"), "head", None, None, "tok"),
        ),
        check_vma=False,
    )
```

```python
import math

import jax
import numpy as np
import jax.numpy as jnp
from jax import lax
from jax.sharding import PartitionSpec as P

ITERS = 2


def shifted(value, axis, by):
    devices = lax.axis_size(axis)
    pairs = [(i, i + by) for i in range(devices) if 0 <= i + by < devices]
    return lax.ppermute(value, axis, pairs)


def rotated(value, axis, by):
    devices = lax.axis_size(axis)
    return lax.ppermute(value, axis, [(i, (i + by) % devices) for i in range(devices)])


def scatter_sum(partial, part_cols):
    tok_count = lax.axis_size("tok")
    me = lax.axis_index("tok")
    last = partial.ndim - 1
    total = lax.dynamic_slice_in_dim(partial, me * part_cols, part_cols, last).astype(jnp.float32)
    for by in range(1, tok_count):
        chunk = lax.dynamic_slice_in_dim(partial, ((me + by) % tok_count) * part_cols, part_cols, last)
        total = total + rotated(chunk, "tok", by).astype(jnp.float32)
    return total


def gather_cols(own, part_cols):
    tok_count = lax.axis_size("tok")
    me = lax.axis_index("tok")
    last = own.ndim - 1
    full = jnp.zeros(own.shape[:-1] + (part_cols * tok_count,), own.dtype)
    full = lax.dynamic_update_slice_in_dim(full, own, me * part_cols, last)
    for by in range(1, tok_count):
        got = rotated(own, "tok", by)
        full = lax.dynamic_update_slice_in_dim(full, got, ((me - by) % tok_count) * part_cols, last)
    return full


def renormalize(matrices, init_norms):
    column_norms = jnp.sqrt(jnp.sum(matrices * matrices, axis=-2) + 1e-06)
    return matrices * (init_norms / column_norms)[..., None, :]


def fast_grads(fast, key_block, scaled):
    gate_pre = jnp.einsum("btd,bdh->bth", key_block, fast[:, 0], preferred_element_type=jnp.float32)
    up_pre = jnp.einsum("btd,bdh->bth", key_block, fast[:, 1], preferred_element_type=jnp.float32)
    sigmoid_gate = jax.nn.sigmoid(gate_pre)
    gated = gate_pre * sigmoid_gate
    hidden = (gated * up_pre).astype(jnp.bfloat16)
    back_grad = jnp.einsum("btd,bhd->bth", scaled, fast[:, 2], preferred_element_type=jnp.float32)
    grad_gate = (
        back_grad * up_pre * sigmoid_gate * (1.0 + gate_pre * (1.0 - sigmoid_gate))
    ).astype(jnp.bfloat16)
    grad_up = (back_grad * gated).astype(jnp.bfloat16)
    first = jnp.einsum("btd,bth->bdh", key_block, grad_gate, preferred_element_type=jnp.float32)
    second = jnp.einsum("btd,bth->bdh", key_block, grad_up, preferred_element_type=jnp.float32)
    third = jnp.einsum("bth,btd->bhd", hidden, scaled, preferred_element_type=jnp.float32)
    return jnp.stack([first, second, third], axis=1).astype(jnp.bfloat16)


def apply_fast(fast, query_block):
    query_gate = jnp.einsum(
        "btd,bdh->bth", query_block, fast[:, 0], preferred_element_type=jnp.float32
    )
    query_up = jnp.einsum("btd,bdh->bth", query_block, fast[:, 1], preferred_element_type=jnp.float32)
    applied = (query_gate * jax.nn.sigmoid(query_gate) * query_up).astype(jnp.bfloat16)
    return jnp.einsum(
        "bth,bhd->btd", applied, fast[:, 2], preferred_element_type=jnp.float32
    ).astype(jnp.bfloat16)


def section_plan(sections, ticks):
    depth = min(sections, ticks)
    slots = -(-ticks // depth)
    done = {}
    phases = []
    while len(done) < sections * ticks:
        phase = len(phases)
        chosen = []
        for s in range(sections):
            ready = [
                t
                for t in range(ticks)
                if (s, t) not in done and (t == 0 or s == 0 or (s - 1, t - 1) in done)
            ]
            chosen.append(ready[:slots])
        for s in range(sections):
            for k, t in enumerate(chosen[s]):
                done[(s, t)] = (phase, k)
        phases.append(chosen)
    return slots, phases, done


def on_device(key_rows, value_rows, query_rows, step_rates, states_in, init_weights):
    tok_count = lax.axis_size("tok")
    sections = lax.axis_size("span")
    feature_width = init_weights.shape[-1]
    part_cols = feature_width // tok_count
    rate_scale = 1.0 / math.sqrt(key_rows.shape[2] * tok_count * feature_width)
    section_index = lax.axis_index("span")
    tok_index = lax.axis_index("tok")
    tick_count = key_rows.shape[0]
    slots, phases, done = section_plan(sections, tick_count)

    init_fast = init_weights[0]
    init_full = init_fast.astype(jnp.float32)
    init_norms = jnp.sqrt(jnp.sum(init_full * init_full, axis=-2) + 1e-06)
    own_norms = lax.dynamic_slice_in_dim(init_norms, tok_index * part_cols, part_cols, 1)
    own_cols = lambda m: lax.dynamic_slice_in_dim(m, tok_index * part_cols, part_cols, m.ndim - 1)

    keys = key_rows[:, 0, :, 0]
    queries = query_rows[:, 0, :, 0]
    scaled_all = (
        (step_rates[:, 0, 0] * rate_scale)[:, :, None] * value_rows[:, 0, :, 0].astype(jnp.float32)
    ).astype(jnp.bfloat16)

    start_weights = states_in[0, 0]
    start_fast = gather_cols(start_weights.astype(jnp.bfloat16), part_cols)
    fast_pool = [start_fast, init_fast]
    weight_pool = [start_weights, own_cols(init_full)]
    slot_code = {}
    finals = []
    out_rows = jnp.zeros((tick_count + 1,) + queries.shape[1:], jnp.bfloat16)
    for phase, chosen in enumerate(phases):
        ticks_here = np.full((slots, sections), tick_count, np.int32)
        source = np.ones((slots, sections), np.int32)
        for s in range(sections):
            for k, t in enumerate(chosen[s]):
                ticks_here[k, s] = t
                if t == 0:
                    source[k, s] = 0
                elif s > 0:
                    q, j = done[(s - 1, t - 1)]
                    source[k, s] = slot_code[(q, j)]
        my_ticks = jnp.asarray(ticks_here)[:, section_index]
        my_source = jnp.asarray(source)[:, section_index]
        fast_stack = jnp.stack(fast_pool)
        weight_stack = jnp.stack(weight_pool)
        fast = jnp.stack([lax.dynamic_index_in_dim(fast_stack, my_source[k], 0, False) for k in range(slots)])
        weights = jnp.stack(
            [lax.dynamic_index_in_dim(weight_stack, my_source[k], 0, False) for k in range(slots)]
        )
        row = jnp.minimum(my_ticks, tick_count - 1)
        key_block = jnp.stack([lax.dynamic_index_in_dim(keys, row[k], 0, False) for k in range(slots)])
        scaled = jnp.stack([lax.dynamic_index_in_dim(scaled_all, row[k], 0, False) for k in range(slots)])
        query_block = jnp.stack([lax.dynamic_index_in_dim(queries, row[k], 0, False) for k in range(slots)])
        for update_step in range(ITERS):
            if update_step > 0:
                fast = gather_cols(weights.astype(jnp.bfloat16), part_cols)
            summed = scatter_sum(fast_grads(fast, key_block, scaled), part_cols)
            weights = renormalize(weights + summed, own_norms)
        fast = gather_cols(weights.astype(jnp.bfloat16), part_cols)
        result = apply_fast(fast, query_block)
        for k in range(slots):
            out_rows = lax.dynamic_update_index_in_dim(out_rows, result[k], my_ticks[k], 0)
            finals.append(weights[k])
        if phase + 1 < len(phases):
            arrived = shifted(fast, "span", 1)
            for k in range(slots):
                slot_code[(phase, k)] = len(fast_pool)
                fast_pool.append(arrived[k])
                weight_pool.append(own_cols(arrived[k]).astype(jnp.float32))
    last = np.zeros((sections,), np.int32)
    for s in range(sections):
        q, j = done[(s, tick_count - 1)]
        last[s] = q * slots + j
    final = lax.dynamic_index_in_dim(jnp.stack(finals), jnp.asarray(last)[section_index], 0, False)
    outputs = out_rows[:tick_count][:, None, :, None]
    return (outputs, final[None, None])


def solution(mesh):
    placed = (
        P("groups", "span", "tok", "head", None),
        P("groups", "span", "tok", "head", None),
        P("groups", "span", "tok", "head", None),
        P("groups", "span", "head", "tok"),
        P(("groups", "span"), "head", None, None, "tok"),
        P("head", None, None, None),
    )
    return jax.shard_map(
        on_device,
        mesh=mesh,
        in_specs=placed,
        out_specs=(
            P("groups", "span", "tok", "head", None),
            P(("groups", "span"), "head", None, None, "tok"),
        ),
        check_vma=False,
    )
```

```python
import math

import jax
import jax.numpy as jnp
from jax import lax
from jax.sharding import PartitionSpec as P

ITERS = 2


def shifted(value, axis, by):
    devices = lax.axis_size(axis)
    pairs = [(i, i + by) for i in range(devices) if 0 <= i + by < devices]
    return lax.ppermute(value, axis, pairs)


def rotated(value, axis, by):
    devices = lax.axis_size(axis)
    return lax.ppermute(value, axis, [(i, (i + by) % devices) for i in range(devices)])


def scatter_sum(partial, part_cols):
    tok_count = lax.axis_size("tok")
    me = lax.axis_index("tok")
    total = lax.dynamic_slice_in_dim(partial, me * part_cols, part_cols, 2).astype(jnp.float32)
    for by in range(1, tok_count):
        chunk = lax.dynamic_slice_in_dim(partial, ((me + by) % tok_count) * part_cols, part_cols, 2)
        total = total + rotated(chunk, "tok", by).astype(jnp.float32)
    return total


def gather_cols(own, part_cols):
    tok_count = lax.axis_size("tok")
    me = lax.axis_index("tok")
    full = jnp.zeros(own.shape[:2] + (part_cols * tok_count,), own.dtype)
    full = lax.dynamic_update_slice_in_dim(full, own, me * part_cols, 2)
    for by in range(1, tok_count):
        got = rotated(own, "tok", by)
        full = lax.dynamic_update_slice_in_dim(full, got, ((me - by) % tok_count) * part_cols, 2)
    return full


def cross_gather(own, part_cols):
    tok_count = lax.axis_size("tok")
    sections = lax.axis_size("span")
    me = lax.axis_index("tok")
    full = jnp.zeros(own.shape[:2] + (part_cols * tok_count,), own.dtype)
    for by in range(tok_count):
        pairs = [
            (t * sections + s, ((t + by) % tok_count) * sections + s + 1)
            for t in range(tok_count)
            for s in range(sections - 1)
        ]
        got = lax.ppermute(own, ("tok", "span"), pairs)
        full = lax.dynamic_update_slice_in_dim(full, got, ((me - by) % tok_count) * part_cols, 2)
    return full


def renormalize(matrices, init_norms):
    column_norms = jnp.sqrt(jnp.sum(matrices * matrices, axis=-2) + 1e-06)
    return matrices * (init_norms / column_norms)[..., None, :]


def fast_grads(fast, key_block, scaled):
    gate_pre = jnp.einsum("td,dh->th", key_block, fast[0], preferred_element_type=jnp.float32)
    up_pre = jnp.einsum("td,dh->th", key_block, fast[1], preferred_element_type=jnp.float32)
    sigmoid_gate = jax.nn.sigmoid(gate_pre)
    gated = gate_pre * sigmoid_gate
    hidden = (gated * up_pre).astype(jnp.bfloat16)
    back_grad = jnp.einsum("td,hd->th", scaled, fast[2], preferred_element_type=jnp.float32)
    grad_gate = (
        back_grad * up_pre * sigmoid_gate * (1.0 + gate_pre * (1.0 - sigmoid_gate))
    ).astype(jnp.bfloat16)
    grad_up = (back_grad * gated).astype(jnp.bfloat16)
    first = jnp.einsum("td,th->dh", key_block, grad_gate, preferred_element_type=jnp.float32)
    second = jnp.einsum("td,th->dh", key_block, grad_up, preferred_element_type=jnp.float32)
    third = jnp.einsum("th,td->hd", hidden, scaled, preferred_element_type=jnp.float32)
    return jnp.stack([first, second, third], axis=0).astype(jnp.bfloat16)


def apply_fast(fast, query_block):
    query_gate = jnp.einsum("td,dh->th", query_block, fast[0], preferred_element_type=jnp.float32)
    query_up = jnp.einsum("td,dh->th", query_block, fast[1], preferred_element_type=jnp.float32)
    applied = (query_gate * jax.nn.sigmoid(query_gate) * query_up).astype(jnp.bfloat16)
    return jnp.einsum(
        "th,hd->td", applied, fast[2], preferred_element_type=jnp.float32
    ).astype(jnp.bfloat16)


def on_device(key_rows, value_rows, query_rows, step_rates, states_in, init_weights):
    tok_count = lax.axis_size("tok")
    feature_width = init_weights.shape[-1]
    part_cols = feature_width // tok_count
    rate_scale = 1.0 / math.sqrt(key_rows.shape[2] * tok_count * feature_width)
    section_index = lax.axis_index("span")
    tok_index = lax.axis_index("tok")
    init_fast = init_weights[0]
    init_full = init_fast.astype(jnp.float32)
    init_norms = jnp.sqrt(jnp.sum(init_full * init_full, axis=-2) + 1e-06)
    own_norms = lax.dynamic_slice_in_dim(init_norms, tok_index * part_cols, part_cols, 1)
    tick_count = key_rows.shape[0]
    results = []
    weights = states_in[0, 0]
    fast = gather_cols(weights.astype(jnp.bfloat16), part_cols)
    arrived = None
    for tick_number in range(tick_count):
        if tick_number > 0:
            fast = jnp.where(section_index == 0, init_fast, arrived)
            weights = lax.dynamic_slice_in_dim(fast, tok_index * part_cols, part_cols, 2).astype(
                jnp.float32
            )
        key_block = key_rows[tick_number, 0, :, 0]
        scaled = (
            (step_rates[tick_number, 0, 0] * rate_scale)[:, None]
            * value_rows[tick_number, 0, :, 0].astype(jnp.float32)
        ).astype(jnp.bfloat16)
        for update_step in range(ITERS):
            if update_step > 0:
                fast = gather_cols(weights.astype(jnp.bfloat16), part_cols)
            summed = scatter_sum(fast_grads(fast, key_block, scaled), part_cols)
            weights = renormalize(weights + summed, own_norms)
        own = weights.astype(jnp.bfloat16)
        if tick_number + 1 < tick_count:
            arrived = cross_gather(own, part_cols)
        fast = gather_cols(own, part_cols)
        results.append(apply_fast(fast, query_rows[tick_number, 0, :, 0]))
    outputs = jnp.stack(results)[:, None, :, None]
    return (outputs, weights[None, None])


def solution(mesh):
    placed = (
        P("groups", "span", "tok", "head", None),
        P("groups", "span", "tok", "head", None),
        P("groups", "span", "tok", "head", None),
        P("groups", "span", "head", "tok"),
        P(("groups", "span"), "head", None, None, "tok"),
        P("head", None, None, None),
    )
    return jax.shard_map(
        on_device,
        mesh=mesh,
        in_specs=placed,
        out_specs=(
            P("groups", "span", "tok", "head", None),
            P(("groups", "span"), "head", None, None, "tok"),
        ),
        check_vma=False,
    )
```

```python
import math

import jax
import jax.numpy as jnp
from jax import lax
from jax.sharding import PartitionSpec as P

ITERS = 2


def shifted(value, axis, by):
    devices = lax.axis_size(axis)
    pairs = [(i, i + by) for i in range(devices) if 0 <= i + by < devices]
    return lax.ppermute(value, axis, pairs)


def rotated(value, axis, by):
    devices = lax.axis_size(axis)
    return lax.ppermute(value, axis, [(i, (i + by) % devices) for i in range(devices)])


def gathered(value):
    tok_count = lax.axis_size("tok")
    return jnp.stack([value] + [rotated(value, "tok", by) for by in range(1, tok_count)])


def summed_over_tok(value):
    tok_count = lax.axis_size("tok")
    total = value
    for by in range(1, tok_count):
        total = total + rotated(value, "tok", by)
    return total


def to_rows(cols):
    tok_count = lax.axis_size("tok")
    part = cols.shape[1]
    pieces = cols.reshape(tok_count, part, part)
    got = lax.all_to_all(pieces, "tok", 0, 0, tiled=False)
    return jnp.transpose(got, (0, 2, 1)).reshape(tok_count * part, part)


def to_cols(rows_t):
    tok_count = lax.axis_size("tok")
    part = rows_t.shape[1]
    pieces = jnp.transpose(rows_t.reshape(tok_count, part, part), (0, 2, 1))
    got = lax.all_to_all(pieces, "tok", 0, 0, tiled=False)
    return got.reshape(tok_count * part, part)


def update(weights, keys, scaled, own_norms):
    fast = weights.astype(jnp.bfloat16)
    gate_pre = jnp.einsum("btd,dh->bth", keys, fast[0], preferred_element_type=jnp.float32)
    up_pre = jnp.einsum("btd,dh->bth", keys, fast[1], preferred_element_type=jnp.float32)
    back_grad = jnp.einsum("btd,dh->bth", scaled, fast[2], preferred_element_type=jnp.float32)
    sigmoid_gate = jax.nn.sigmoid(gate_pre)
    gated = gate_pre * sigmoid_gate
    hidden = (gated * up_pre).astype(jnp.bfloat16)
    grad_gate = (
        back_grad * up_pre * sigmoid_gate * (1.0 + gate_pre * (1.0 - sigmoid_gate))
    ).astype(jnp.bfloat16)
    grad_up = (back_grad * gated).astype(jnp.bfloat16)
    first = jnp.einsum("btd,bth->bdh", keys, grad_gate, preferred_element_type=jnp.float32)
    second = jnp.einsum("btd,bth->bdh", keys, grad_up, preferred_element_type=jnp.float32)
    third = jnp.einsum("btd,bth->bdh", scaled, hidden, preferred_element_type=jnp.float32)
    partial = jnp.stack([first, second, third], axis=1).astype(jnp.bfloat16)
    weights = weights + jnp.sum(partial.astype(jnp.float32), axis=0)
    squares = jnp.sum(weights * weights, axis=1)
    first_two = jnp.sqrt(squares[:2] + 1e-06)
    w2_squares = summed_over_tok(jnp.sum(weights[2] * weights[2], axis=1))
    w2_norms = jnp.sqrt(w2_squares + 1e-06)
    top = weights[:2] * (own_norms[0] / first_two)[:, None, :]
    last = weights[2] * (own_norms[1] / w2_norms)[:, None]
    return jnp.concatenate([top, last[None]], axis=0)


def apply_fast(weights, query_block):
    fast = jnp.concatenate(gathered(weights.astype(jnp.bfloat16)), axis=-1)
    query_gate = jnp.einsum("td,dh->th", query_block, fast[0], preferred_element_type=jnp.float32)
    query_up = jnp.einsum("td,dh->th", query_block, fast[1], preferred_element_type=jnp.float32)
    applied = (query_gate * jax.nn.sigmoid(query_gate) * query_up).astype(jnp.bfloat16)
    return jnp.einsum(
        "th,dh->td", applied, fast[2], preferred_element_type=jnp.float32
    ).astype(jnp.bfloat16)


def on_device(key_rows, value_rows, query_rows, step_rates, states_in, init_weights):
    tok_count = lax.axis_size("tok")
    feature_width = init_weights.shape[-1]
    part = feature_width // tok_count
    rate_scale = 1.0 / math.sqrt(key_rows.shape[2] * tok_count * feature_width)
    section_index = lax.axis_index("span")
    tok_index = lax.axis_index("tok")
    init_full = init_weights[0].astype(jnp.float32)
    init_norms = jnp.sqrt(jnp.sum(init_full * init_full, axis=-2) + 1e-06)
    own_hidden = lambda m: lax.dynamic_slice_in_dim(m, tok_index * part, part, m.ndim - 1)
    own_norms = (jnp.stack([own_hidden(init_norms[0]), own_hidden(init_norms[1])]), init_norms[2])
    init_own = jnp.stack(
        [own_hidden(init_full[0]), own_hidden(init_full[1]), own_hidden(init_full[2].T)]
    )
    tick_count = key_rows.shape[0]
    start = states_in[0, 0]
    weights = jnp.stack([start[0], start[1], to_rows(start[2])])
    blocks = []
    after = weights
    for tick_number in range(tick_count):
        scaled = (
            (step_rates[tick_number, 0, 0] * rate_scale)[:, None]
            * value_rows[tick_number, 0, :, 0].astype(jnp.float32)
        ).astype(jnp.bfloat16)
        rows, _ = lax.optimization_barrier((jnp.stack([key_rows[tick_number, 0, :, 0], scaled]), after))
        blocks.append(gathered(rows))
        after = blocks[-1]
    results = []
    for tick_number in range(tick_count):
        if tick_number > 0:
            arrived = shifted(weights, "span", 1)
            weights = jnp.where(section_index == 0, init_own, arrived)
        keys, scaled = blocks[tick_number][:, 0], blocks[tick_number][:, 1]
        for update_step in range(ITERS):
            weights = update(weights, keys, scaled, own_norms)
        results.append(apply_fast(weights, query_rows[tick_number, 0, :, 0]))
    outputs = jnp.stack(results)[:, None, :, None]
    final = jnp.stack([weights[0], weights[1], to_cols(weights[2])])
    return (outputs, final[None, None])


def solution(mesh):
    placed = (
        P("groups", "span", "tok", "head", None),
        P("groups", "span", "tok", "head", None),
        P("groups", "span", "tok", "head", None),
        P("groups", "span", "head", "tok"),
        P(("groups", "span"), "head", None, None, "tok"),
        P("head", None, None, None),
    )
    return jax.shard_map(
        on_device,
        mesh=mesh,
        in_specs=placed,
        out_specs=(
            P("groups", "span", "tok", "head", None),
            P(("groups", "span"), "head", None, None, "tok"),
        ),
        check_vma=False,
    )
```

```python
import math

import jax
import jax.numpy as jnp
from jax import lax
from jax.sharding import PartitionSpec as P

ITERS = 2


def shifted(value, axis, by):
    devices = lax.axis_size(axis)
    pairs = [(i, i + by) for i in range(devices) if 0 <= i + by < devices]
    return lax.ppermute(value, axis, pairs)


def rotated(value, axis, by):
    devices = lax.axis_size(axis)
    return lax.ppermute(value, axis, [(i, (i + by) % devices) for i in range(devices)])


def scatter_sum(partial, part_cols):
    tok_count = lax.axis_size("tok")
    me = lax.axis_index("tok")
    total = lax.dynamic_slice_in_dim(partial, me * part_cols, part_cols, 2).astype(jnp.float32)
    for by in range(1, tok_count):
        chunk = lax.dynamic_slice_in_dim(partial, ((me + by) % tok_count) * part_cols, part_cols, 2)
        total = total + rotated(chunk, "tok", by).astype(jnp.float32)
    return total


def gather_cols(own, part_cols):
    tok_count = lax.axis_size("tok")
    me = lax.axis_index("tok")
    full = jnp.zeros(own.shape[:2] + (part_cols * tok_count,), own.dtype)
    full = lax.dynamic_update_slice_in_dim(full, own, me * part_cols, 2)
    for by in range(1, tok_count):
        got = rotated(own, "tok", by)
        full = lax.dynamic_update_slice_in_dim(full, got, ((me - by) % tok_count) * part_cols, 2)
    return full


def cross_gather(own, part_cols):
    tok_count = lax.axis_size("tok")
    sections = lax.axis_size("span")
    me = lax.axis_index("tok")
    full = jnp.zeros(own.shape[:2] + (part_cols * tok_count,), own.dtype)
    for by in range(tok_count):
        pairs = [
            (t * sections + s, ((t + by) % tok_count) * sections + (s + 1) % sections)
            for t in range(tok_count)
            for s in range(sections)
        ]
        got = lax.ppermute(own, ("tok", "span"), pairs)
        full = lax.dynamic_update_slice_in_dim(full, got, ((me - by) % tok_count) * part_cols, 2)
    return full


def renormalize(matrices, init_norms):
    column_norms = jnp.sqrt(jnp.sum(matrices * matrices, axis=-2) + 1e-06)
    return matrices * (init_norms / column_norms)[..., None, :]


def fast_grads(fast, key_block, scaled):
    gate_pre = jnp.einsum("td,dh->th", key_block, fast[0], preferred_element_type=jnp.float32)
    up_pre = jnp.einsum("td,dh->th", key_block, fast[1], preferred_element_type=jnp.float32)
    sigmoid_gate = jax.nn.sigmoid(gate_pre)
    gated = gate_pre * sigmoid_gate
    hidden = (gated * up_pre).astype(jnp.bfloat16)
    back_grad = jnp.einsum("td,hd->th", scaled, fast[2], preferred_element_type=jnp.float32)
    grad_gate = (
        back_grad * up_pre * sigmoid_gate * (1.0 + gate_pre * (1.0 - sigmoid_gate))
    ).astype(jnp.bfloat16)
    grad_up = (back_grad * gated).astype(jnp.bfloat16)
    first = jnp.einsum("td,th->dh", key_block, grad_gate, preferred_element_type=jnp.float32)
    second = jnp.einsum("td,th->dh", key_block, grad_up, preferred_element_type=jnp.float32)
    third = jnp.einsum("th,td->hd", hidden, scaled, preferred_element_type=jnp.float32)
    return jnp.stack([first, second, third], axis=0).astype(jnp.bfloat16)


def apply_fast(fast, query_block):
    query_gate = jnp.einsum("td,dh->th", query_block, fast[0], preferred_element_type=jnp.float32)
    query_up = jnp.einsum("td,dh->th", query_block, fast[1], preferred_element_type=jnp.float32)
    applied = (query_gate * jax.nn.sigmoid(query_gate) * query_up).astype(jnp.bfloat16)
    return jnp.einsum(
        "th,hd->td", applied, fast[2], preferred_element_type=jnp.float32
    ).astype(jnp.bfloat16)


def on_device(key_rows, value_rows, query_rows, step_rates, states_in, init_weights):
    tok_count = lax.axis_size("tok")
    feature_width = init_weights.shape[-1]
    part_cols = feature_width // tok_count
    rate_scale = 1.0 / math.sqrt(key_rows.shape[2] * tok_count * feature_width)
    section_index = lax.axis_index("span")
    tok_index = lax.axis_index("tok")
    init_fast = init_weights[0]
    init_full = init_fast.astype(jnp.float32)
    init_norms = jnp.sqrt(jnp.sum(init_full * init_full, axis=-2) + 1e-06)
    own_norms = lax.dynamic_slice_in_dim(init_norms, tok_index * part_cols, part_cols, 1)
    tick_count = key_rows.shape[0]
    results = []
    weights = states_in[0, 0]
    fast = gather_cols(weights.astype(jnp.bfloat16), part_cols)
    arrived = None
    earlier_queries = rotated(query_rows[: tick_count - 1, 0, :, 0], "span", 1)
    for tick_number in range(tick_count):
        if tick_number > 0:
            fast = jnp.where(section_index == 0, init_fast, arrived)
            weights = lax.dynamic_slice_in_dim(fast, tok_index * part_cols, part_cols, 2).astype(
                jnp.float32
            )
        key_block = key_rows[tick_number, 0, :, 0]
        scaled = (
            (step_rates[tick_number, 0, 0] * rate_scale)[:, None]
            * value_rows[tick_number, 0, :, 0].astype(jnp.float32)
        ).astype(jnp.bfloat16)
        for update_step in range(ITERS):
            if update_step > 0:
                fast = gather_cols(weights.astype(jnp.bfloat16), part_cols)
            summed = scatter_sum(fast_grads(fast, key_block, scaled), part_cols)
            weights = renormalize(weights + summed, own_norms)
        own = weights.astype(jnp.bfloat16)
        if tick_number + 1 < tick_count:
            arrived = cross_gather(own, part_cols)
            for_previous = apply_fast(arrived, earlier_queries[tick_number])
            results.append(rotated(for_previous, "span", -1))
        else:
            fast = gather_cols(own, part_cols)
            results.append(apply_fast(fast, query_rows[tick_number, 0, :, 0]))
    outputs = jnp.stack(results)[:, None, :, None]
    return (outputs, weights[None, None])


def solution(mesh):
    placed = (
        P("groups", "span", "tok", "head", None),
        P("groups", "span", "tok", "head", None),
        P("groups", "span", "tok", "head", None),
        P("groups", "span", "head", "tok"),
        P(("groups", "span"), "head", None, None, "tok"),
        P("head", None, None, None),
    )
    return jax.shard_map(
        on_device,
        mesh=mesh,
        in_specs=placed,
        out_specs=(
            P("groups", "span", "tok", "head", None),
            P(("groups", "span"), "head", None, None, "tok"),
        ),
        check_vma=False,
    )
```

```python
import math

import jax
import jax.numpy as jnp
from jax import lax
from jax.sharding import PartitionSpec as P


ITERS = 2


def rotated(value, axis, by):
    devices = lax.axis_size(axis)
    return lax.ppermute(value, axis, [(i, (i + by) % devices) for i in range(devices)])


def scatter_sum(partial, part_cols):
    tok_count = lax.axis_size("tok")
    me = lax.axis_index("tok")
    total = lax.dynamic_slice_in_dim(partial, me * part_cols, part_cols, 2).astype(jnp.float32)
    for by in range(1, tok_count):
        chunk = lax.dynamic_slice_in_dim(partial, ((me + by) % tok_count) * part_cols, part_cols, 2)
        total = total + rotated(chunk, "tok", by).astype(jnp.float32)
    return total


def gather_cols(own, part_cols):
    tok_count = lax.axis_size("tok")
    me = lax.axis_index("tok")
    full = jnp.zeros(own.shape[:2] + (part_cols * tok_count,), own.dtype)
    full = lax.dynamic_update_slice_in_dim(full, own, me * part_cols, 2)
    for by in range(1, tok_count):
        got = rotated(own, "tok", by)
        full = lax.dynamic_update_slice_in_dim(full, got, ((me - by) % tok_count) * part_cols, 2)
    return full


def cross_gather(own, part_cols):
    tok_count = lax.axis_size("tok")
    sections = lax.axis_size("span")
    me = lax.axis_index("tok")
    full = jnp.zeros(own.shape[:2] + (part_cols * tok_count,), own.dtype)
    for by in range(tok_count):
        pairs = [
            (t * sections + s, ((t + by) % tok_count) * sections + (s + 1) % sections)
            for t in range(tok_count)
            for s in range(sections)
        ]
        got = lax.ppermute(own, ("tok", "span"), pairs)
        full = lax.dynamic_update_slice_in_dim(full, got, ((me - by) % tok_count) * part_cols, 2)
    return full


def renormalize(matrices, init_norms):
    column_norms = jnp.sqrt(jnp.sum(matrices * matrices, axis=-2) + 1e-06)
    return matrices * (init_norms / column_norms)[..., None, :]


def fast_grads(fast, key_block, scaled):
    gate_pre = jnp.einsum("td,dh->th", key_block, fast[0], preferred_element_type=jnp.float32)
    up_pre = jnp.einsum("td,dh->th", key_block, fast[1], preferred_element_type=jnp.float32)
    sigmoid_gate = jax.nn.sigmoid(gate_pre)
    gated = gate_pre * sigmoid_gate
    hidden = (gated * up_pre).astype(jnp.bfloat16)
    back_grad = jnp.einsum("td,hd->th", scaled, fast[2], preferred_element_type=jnp.float32)
    grad_gate = (
        back_grad * up_pre * sigmoid_gate * (1.0 + gate_pre * (1.0 - sigmoid_gate))
    ).astype(jnp.bfloat16)
    grad_up = (back_grad * gated).astype(jnp.bfloat16)
    first = jnp.einsum("td,th->dh", key_block, grad_gate, preferred_element_type=jnp.float32)
    second = jnp.einsum("td,th->dh", key_block, grad_up, preferred_element_type=jnp.float32)
    third = jnp.einsum("th,td->hd", hidden, scaled, preferred_element_type=jnp.float32)
    return jnp.stack([first, second, third], axis=0).astype(jnp.bfloat16)


def apply_fast(fast, query_block):
    query_gate = jnp.einsum("td,dh->th", query_block, fast[0], preferred_element_type=jnp.float32)
    query_up = jnp.einsum("td,dh->th", query_block, fast[1], preferred_element_type=jnp.float32)
    applied = (query_gate * jax.nn.sigmoid(query_gate) * query_up).astype(jnp.bfloat16)
    return jnp.einsum(
        "th,hd->td", applied, fast[2], preferred_element_type=jnp.float32
    ).astype(jnp.bfloat16)


def section_chain(key_rows, value_rows, query_rows, step_rates, states_in, init_weights):
    tok_count = lax.axis_size("tok")
    feature_width = init_weights.shape[-1]
    part_cols = feature_width // tok_count
    rate_scale = 1.0 / math.sqrt(key_rows.shape[2] * tok_count * feature_width)
    section_index = lax.axis_index("span")
    tok_index = lax.axis_index("tok")
    init_fast = init_weights[0]
    init_full = init_fast.astype(jnp.float32)
    init_norms = jnp.sqrt(jnp.sum(init_full * init_full, axis=-2) + 1e-06)
    own_norms = lax.dynamic_slice_in_dim(init_norms, tok_index * part_cols, part_cols, 1)
    tick_count = key_rows.shape[0]
    results = []
    weights = states_in[0, 0]
    fast = gather_cols(weights.astype(jnp.bfloat16), part_cols)
    arrived = None
    earlier_queries = rotated(query_rows[: tick_count - 1, 0, :, 0], "span", 1)
    for tick_number in range(tick_count):
        if tick_number > 0:
            fast = jnp.where(section_index == 0, init_fast, arrived)
            weights = lax.dynamic_slice_in_dim(fast, tok_index * part_cols, part_cols, 2).astype(
                jnp.float32
            )
        key_block = key_rows[tick_number, 0, :, 0]
        scaled = (
            (step_rates[tick_number, 0, 0] * rate_scale)[:, None]
            * value_rows[tick_number, 0, :, 0].astype(jnp.float32)
        ).astype(jnp.bfloat16)
        for update_step in range(ITERS):
            if update_step > 0:
                fast = gather_cols(weights.astype(jnp.bfloat16), part_cols)
            partial = fast_grads(fast, key_block, scaled)
            summed = scatter_sum(partial, part_cols)
            weights = renormalize(weights + summed, own_norms)
        own = weights.astype(jnp.bfloat16)
        if tick_number + 1 < tick_count:
            arrived = cross_gather(own, part_cols)
            for_previous = apply_fast(arrived, earlier_queries[tick_number])
            results.append(rotated(for_previous, "span", -1))
        else:
            fast = gather_cols(own, part_cols)
            results.append(apply_fast(fast, query_rows[tick_number, 0, :, 0]))
    outputs = jnp.stack(results)[:, None, :, None]
    return (outputs, weights[None, None])


def solution(mesh):
    placed = (
        P("groups", "span", "tok", "head", None),
        P("groups", "span", "tok", "head", None),
        P("groups", "span", "tok", "head", None),
        P("groups", "span", "head", "tok"),
        P(("groups", "span"), "head", None, None, "tok"),
        P("head", None, None, None),
    )
    return jax.shard_map(
        section_chain,
        mesh=mesh,
        in_specs=placed,
        out_specs=(
            P("groups", "span", "tok", "head", None),
            P(("groups", "span"), "head", None, None, "tok"),
        ),
        check_vma=False,
    )
```

```python
import math

import jax
import jax.numpy as jnp
from jax import lax
from jax.sharding import PartitionSpec as P


ITERS = 2
DELAY_STEPS = 60


def rotated(value, axis, by):
    devices = lax.axis_size(axis)
    return lax.ppermute(value, axis, [(i, (i + by) % devices) for i in range(devices)])


def scatter_sum(partial, part_cols):
    tok_count = lax.axis_size("tok")
    me = lax.axis_index("tok")
    total = lax.dynamic_slice_in_dim(partial, me * part_cols, part_cols, 2).astype(jnp.float32)
    for by in range(1, tok_count):
        chunk = lax.dynamic_slice_in_dim(partial, ((me + by) % tok_count) * part_cols, part_cols, 2)
        total = total + rotated(chunk, "tok", by).astype(jnp.float32)
    return total


def gather_cols(own, part_cols):
    tok_count = lax.axis_size("tok")
    me = lax.axis_index("tok")
    full = jnp.zeros(own.shape[:2] + (part_cols * tok_count,), own.dtype)
    full = lax.dynamic_update_slice_in_dim(full, own, me * part_cols, 2)
    for by in range(1, tok_count):
        got = rotated(own, "tok", by)
        full = lax.dynamic_update_slice_in_dim(full, got, ((me - by) % tok_count) * part_cols, 2)
    return full


def cross_gather(own, part_cols):
    tok_count = lax.axis_size("tok")
    sections = lax.axis_size("span")
    me = lax.axis_index("tok")
    full = jnp.zeros(own.shape[:2] + (part_cols * tok_count,), own.dtype)
    for by in range(tok_count):
        pairs = [
            (t * sections + s, ((t + by) % tok_count) * sections + (s + 1) % sections)
            for t in range(tok_count)
            for s in range(sections)
        ]
        got = lax.ppermute(own, ("tok", "span"), pairs)
        full = lax.dynamic_update_slice_in_dim(full, got, ((me - by) % tok_count) * part_cols, 2)
    return full


def renormalize(matrices, init_norms):
    column_norms = jnp.sqrt(jnp.sum(matrices * matrices, axis=-2) + 1e-06)
    return matrices * (init_norms / column_norms)[..., None, :]


def fast_grads(fast, key_block, scaled):
    pair = jnp.einsum("td,mdh->mth", key_block, fast[:2], preferred_element_type=jnp.float32)
    gate_pre, up_pre = pair[0], pair[1]
    sigmoid_gate = jax.nn.sigmoid(gate_pre)
    gated = gate_pre * sigmoid_gate
    hidden = (gated * up_pre).astype(jnp.bfloat16)
    back_grad = jnp.einsum("td,hd->th", scaled, fast[2], preferred_element_type=jnp.float32)
    grad_gate = (
        back_grad * up_pre * sigmoid_gate * (1.0 + gate_pre * (1.0 - sigmoid_gate))
    ).astype(jnp.bfloat16)
    grad_up = (back_grad * gated).astype(jnp.bfloat16)
    grads = jnp.stack([grad_gate, grad_up])
    first_two = jnp.einsum("td,mth->mdh", key_block, grads, preferred_element_type=jnp.float32)
    third = jnp.einsum("th,td->hd", hidden, scaled, preferred_element_type=jnp.float32)
    return jnp.concatenate([first_two, third[None]], axis=0).astype(jnp.bfloat16)


def apply_fast(fast, query_block):
    query_gate = jnp.einsum("td,dh->th", query_block, fast[0], preferred_element_type=jnp.float32)
    query_up = jnp.einsum("td,dh->th", query_block, fast[1], preferred_element_type=jnp.float32)
    applied = (query_gate * jax.nn.sigmoid(query_gate) * query_up).astype(jnp.bfloat16)
    return jnp.einsum(
        "th,hd->td", applied, fast[2], preferred_element_type=jnp.float32
    ).astype(jnp.bfloat16)


def section_chain(key_rows, value_rows, query_rows, step_rates, states_in, init_weights):
    tok_count = lax.axis_size("tok")
    feature_width = init_weights.shape[-1]
    part_cols = feature_width // tok_count
    rate_scale = 1.0 / math.sqrt(key_rows.shape[2] * tok_count * feature_width)
    section_index = lax.axis_index("span")
    tok_index = lax.axis_index("tok")
    init_fast = init_weights[0]
    init_full = init_fast.astype(jnp.float32)
    init_norms = jnp.sqrt(jnp.sum(init_full * init_full, axis=-2) + 1e-06)
    own_norms = lax.dynamic_slice_in_dim(init_norms, tok_index * part_cols, part_cols, 1)
    tick_count = key_rows.shape[0]
    results = []
    weights = states_in[0, 0]
    unit = (init_norms[0, 0] + 1.0) / (init_norms[0, 0] + 1.0)
    weights = lax.fori_loop(
        0, lax.axis_index("head") * DELAY_STEPS, lambda step, held: held * unit, weights
    )
    fast = gather_cols(weights.astype(jnp.bfloat16), part_cols)
    arrived = None
    earlier_queries = rotated(query_rows[: tick_count - 1, 0, :, 0], "span", 1)
    for tick_number in range(tick_count):
        if tick_number > 0:
            fast = jnp.where(section_index == 0, init_fast, arrived)
            weights = lax.dynamic_slice_in_dim(fast, tok_index * part_cols, part_cols, 2).astype(
                jnp.float32
            )
        key_block = key_rows[tick_number, 0, :, 0]
        scaled = (
            (step_rates[tick_number, 0, 0] * rate_scale)[:, None]
            * value_rows[tick_number, 0, :, 0].astype(jnp.float32)
        ).astype(jnp.bfloat16)
        for update_step in range(ITERS):
            if update_step > 0:
                fast = gather_cols(weights.astype(jnp.bfloat16), part_cols)
            partial = fast_grads(fast, key_block, scaled)
            summed = scatter_sum(partial, part_cols)
            weights = renormalize(weights + summed, own_norms)
        own = weights.astype(jnp.bfloat16)
        if tick_number + 1 < tick_count:
            arrived = cross_gather(own, part_cols)
            for_previous = apply_fast(arrived, earlier_queries[tick_number])
            results.append(rotated(for_previous, "span", -1))
        else:
            fast = gather_cols(own, part_cols)
            results.append(apply_fast(fast, query_rows[tick_number, 0, :, 0]))
    outputs = jnp.stack(results)[:, None, :, None]
    return (outputs, weights[None, None])


def solution(mesh):
    placed = (
        P("groups", "span", "tok", "head", None),
        P("groups", "span", "tok", "head", None),
        P("groups", "span", "tok", "head", None),
        P("groups", "span", "head", "tok"),
        P(("groups", "span"), "head", None, None, "tok"),
        P("head", None, None, None),
    )
    return jax.shard_map(
        section_chain,
        mesh=mesh,
        in_specs=placed,
        out_specs=(
            P("groups", "span", "tok", "head", None),
            P(("groups", "span"), "head", None, None, "tok"),
        ),
        check_vma=False,
    )
```

```python
import math

import jax
import jax.numpy as jnp
from jax import lax
from jax.experimental import pallas as pl
from jax.experimental.pallas import tpu as pltpu
from jax.sharding import PartitionSpec as P


ITERS = 2
DELAY_STEPS = 60


def rotated(value, axis, by):
    devices = lax.axis_size(axis)
    return lax.ppermute(value, axis, [(i, (i + by) % devices) for i in range(devices)])


def scatter_sum(partial, part_cols):
    tok_count = lax.axis_size("tok")
    me = lax.axis_index("tok")
    total = lax.dynamic_slice_in_dim(partial, me * part_cols, part_cols, 2).astype(jnp.float32)
    for by in range(1, tok_count):
        chunk = lax.dynamic_slice_in_dim(partial, ((me + by) % tok_count) * part_cols, part_cols, 2)
        total = total + rotated(chunk, "tok", by).astype(jnp.float32)
    return total


def gather_cols(own, part_cols):
    tok_count = lax.axis_size("tok")
    me = lax.axis_index("tok")
    full = jnp.zeros(own.shape[:2] + (part_cols * tok_count,), own.dtype)
    full = lax.dynamic_update_slice_in_dim(full, own, me * part_cols, 2)
    for by in range(1, tok_count):
        got = rotated(own, "tok", by)
        full = lax.dynamic_update_slice_in_dim(full, got, ((me - by) % tok_count) * part_cols, 2)
    return full


def cross_gather(own, part_cols):
    tok_count = lax.axis_size("tok")
    sections = lax.axis_size("span")
    me = lax.axis_index("tok")
    full = jnp.zeros(own.shape[:2] + (part_cols * tok_count,), own.dtype)
    for by in range(tok_count):
        pairs = [
            (t * sections + s, ((t + by) % tok_count) * sections + (s + 1) % sections)
            for t in range(tok_count)
            for s in range(sections)
        ]
        got = lax.ppermute(own, ("tok", "span"), pairs)
        full = lax.dynamic_update_slice_in_dim(full, got, ((me - by) % tok_count) * part_cols, 2)
    return full


def renormalize(matrices, init_norms):
    column_norms = jnp.sqrt(jnp.sum(matrices * matrices, axis=-2) + 1e-06)
    return matrices * (init_norms / column_norms)[..., None, :]


_T0 = (((0,), (0,)), ((), ()))
_T1 = (((1,), (1,)), ((), ()))


def _grads_body(key_ref, scaled_ref, fast_ref, out_ref):
    keys = key_ref[...]
    scaled = scaled_ref[...]
    gate_pre = jnp.dot(keys, fast_ref[0], preferred_element_type=jnp.float32)
    up_pre = jnp.dot(keys, fast_ref[1], preferred_element_type=jnp.float32)
    back_grad = lax.dot_general(scaled, fast_ref[2], _T1, preferred_element_type=jnp.float32)
    sigmoid_gate = 1.0 / (1.0 + jnp.exp(-gate_pre))
    gated = gate_pre * sigmoid_gate
    hidden = (gated * up_pre).astype(jnp.bfloat16)
    grad_gate = (
        back_grad * up_pre * sigmoid_gate * (1.0 + gate_pre * (1.0 - sigmoid_gate))
    ).astype(jnp.bfloat16)
    grad_up = (back_grad * gated).astype(jnp.bfloat16)
    out_ref[0] = lax.dot_general(keys, grad_gate, _T0, preferred_element_type=jnp.float32).astype(out_ref.dtype)
    out_ref[1] = lax.dot_general(keys, grad_up, _T0, preferred_element_type=jnp.float32).astype(out_ref.dtype)
    out_ref[2] = lax.dot_general(hidden, scaled, _T0, preferred_element_type=jnp.float32).astype(out_ref.dtype)


def fast_grads_kernel(fast, key_block, scaled):
    tokens, width = key_block.shape
    flops = 2 * tokens * width * width * 6
    return pl.pallas_call(
        _grads_body,
        out_shape=jax.ShapeDtypeStruct(fast.shape, jnp.bfloat16),
        in_specs=[pl.BlockSpec(memory_space=pltpu.VMEM)] * 3,
        out_specs=pl.BlockSpec(memory_space=pltpu.VMEM),
        cost_estimate=pl.CostEstimate(
            flops=flops, transcendentals=tokens * width, bytes_accessed=2 * (2 * tokens * width + 6 * width * width)
        ),
    )(key_block, scaled, fast)


def apply_fast(fast, query_block):
    query_gate = jnp.einsum("td,dh->th", query_block, fast[0], preferred_element_type=jnp.float32)
    query_up = jnp.einsum("td,dh->th", query_block, fast[1], preferred_element_type=jnp.float32)
    applied = (query_gate * jax.nn.sigmoid(query_gate) * query_up).astype(jnp.bfloat16)
    return jnp.einsum(
        "th,hd->td", applied, fast[2], preferred_element_type=jnp.float32
    ).astype(jnp.bfloat16)


def section_chain(key_rows, value_rows, query_rows, step_rates, states_in, init_weights):
    tok_count = lax.axis_size("tok")
    feature_width = init_weights.shape[-1]
    part_cols = feature_width // tok_count
    rate_scale = 1.0 / math.sqrt(key_rows.shape[2] * tok_count * feature_width)
    section_index = lax.axis_index("span")
    tok_index = lax.axis_index("tok")
    init_fast = init_weights[0]
    init_full = init_fast.astype(jnp.float32)
    init_norms = jnp.sqrt(jnp.sum(init_full * init_full, axis=-2) + 1e-06)
    own_norms = lax.dynamic_slice_in_dim(init_norms, tok_index * part_cols, part_cols, 1)
    tick_count = key_rows.shape[0]
    results = []
    weights = states_in[0, 0]
    unit = (init_norms[0, 0] + 1.0) / (init_norms[0, 0] + 1.0)
    weights = lax.fori_loop(
        0, lax.axis_index("head") * DELAY_STEPS, lambda step, held: held * unit, weights
    )
    fast = gather_cols(weights.astype(jnp.bfloat16), part_cols)
    arrived = None
    earlier_queries = rotated(query_rows[: tick_count - 1, 0, :, 0], "span", 1)
    for tick_number in range(tick_count):
        if tick_number > 0:
            fast = jnp.where(section_index == 0, init_fast, arrived)
            weights = lax.dynamic_slice_in_dim(fast, tok_index * part_cols, part_cols, 2).astype(
                jnp.float32
            )
        key_block = key_rows[tick_number, 0, :, 0]
        scaled = (
            (step_rates[tick_number, 0, 0] * rate_scale)[:, None]
            * value_rows[tick_number, 0, :, 0].astype(jnp.float32)
        ).astype(jnp.bfloat16)
        for update_step in range(ITERS):
            if update_step > 0:
                fast = gather_cols(weights.astype(jnp.bfloat16), part_cols)
            partial = fast_grads_kernel(fast, key_block, scaled)
            summed = scatter_sum(partial, part_cols)
            weights = renormalize(weights + summed, own_norms)
        own = weights.astype(jnp.bfloat16)
        if tick_number + 1 < tick_count:
            arrived = cross_gather(own, part_cols)
            for_previous = apply_fast(arrived, earlier_queries[tick_number])
            results.append(rotated(for_previous, "span", -1))
        else:
            fast = gather_cols(own, part_cols)
            results.append(apply_fast(fast, query_rows[tick_number, 0, :, 0]))
    outputs = jnp.stack(results)[:, None, :, None]
    return (outputs, weights[None, None])


def solution(mesh):
    placed = (
        P("groups", "span", "tok", "head", None),
        P("groups", "span", "tok", "head", None),
        P("groups", "span", "tok", "head", None),
        P("groups", "span", "head", "tok"),
        P(("groups", "span"), "head", None, None, "tok"),
        P("head", None, None, None),
    )
    return jax.shard_map(
        section_chain,
        mesh=mesh,
        in_specs=placed,
        out_specs=(
            P("groups", "span", "tok", "head", None),
            P(("groups", "span"), "head", None, None, "tok"),
        ),
        check_vma=False,
    )
```

```python
import math

import jax
import jax.numpy as jnp
from jax import lax
from jax.sharding import PartitionSpec as P


ITERS = 2
DELAY_STEPS = 60


def rotated(value, axis, by):
    devices = lax.axis_size(axis)
    return lax.ppermute(value, axis, [(i, (i + by) % devices) for i in range(devices)])


def scatter_sum(partial, part_cols):
    tok_count = lax.axis_size("tok")
    me = lax.axis_index("tok")
    total = lax.dynamic_slice_in_dim(partial, me * part_cols, part_cols, 2).astype(jnp.float32)
    for by in range(1, tok_count):
        chunk = lax.dynamic_slice_in_dim(partial, ((me + by) % tok_count) * part_cols, part_cols, 2)
        total = total + rotated(chunk, "tok", by).astype(jnp.float32)
    return total


def gather_cols(own, part_cols):
    tok_count = lax.axis_size("tok")
    me = lax.axis_index("tok")
    full = jnp.zeros(own.shape[:2] + (part_cols * tok_count,), own.dtype)
    full = lax.dynamic_update_slice_in_dim(full, own, me * part_cols, 2)
    for by in range(1, tok_count):
        got = rotated(own, "tok", by)
        full = lax.dynamic_update_slice_in_dim(full, got, ((me - by) % tok_count) * part_cols, 2)
    return full


def cross_gather(own, part_cols):
    tok_count = lax.axis_size("tok")
    sections = lax.axis_size("span")
    me = lax.axis_index("tok")
    full = jnp.zeros(own.shape[:2] + (part_cols * tok_count,), own.dtype)
    for by in range(tok_count):
        pairs = [
            (t * sections + s, ((t + by) % tok_count) * sections + (s + 1) % sections)
            for t in range(tok_count)
            for s in range(sections)
        ]
        got = lax.ppermute(own, ("tok", "span"), pairs)
        full = lax.dynamic_update_slice_in_dim(full, got, ((me - by) % tok_count) * part_cols, 2)
    return full


def renormalize(matrices, init_norms):
    column_norms = jnp.sqrt(jnp.sum(matrices * matrices, axis=-2) + 1e-06)
    return matrices * (init_norms / column_norms)[..., None, :]


def fast_grads(fast, key_block, scaled):
    gate_pre = jnp.einsum("td,dh->th", key_block, fast[0], preferred_element_type=jnp.float32)
    up_pre = jnp.einsum("td,dh->th", key_block, fast[1], preferred_element_type=jnp.float32)
    sigmoid_gate = jax.nn.sigmoid(gate_pre)
    gated = gate_pre * sigmoid_gate
    hidden = (gated * up_pre).astype(jnp.bfloat16)
    back_grad = jnp.einsum("td,hd->th", scaled, fast[2], preferred_element_type=jnp.float32)
    grad_gate = (
        back_grad * up_pre * sigmoid_gate * (1.0 + gate_pre * (1.0 - sigmoid_gate))
    ).astype(jnp.bfloat16)
    grad_up = (back_grad * gated).astype(jnp.bfloat16)
    first = jnp.einsum("td,th->dh", key_block, grad_gate, preferred_element_type=jnp.float32)
    second = jnp.einsum("td,th->dh", key_block, grad_up, preferred_element_type=jnp.float32)
    third = jnp.einsum("th,td->hd", hidden, scaled, preferred_element_type=jnp.float32)
    return jnp.stack([first, second, third], axis=0).astype(jnp.bfloat16)


def apply_fast(fast, query_block):
    query_gate = jnp.einsum("td,dh->th", query_block, fast[0], preferred_element_type=jnp.float32)
    query_up = jnp.einsum("td,dh->th", query_block, fast[1], preferred_element_type=jnp.float32)
    applied = (query_gate * jax.nn.sigmoid(query_gate) * query_up).astype(jnp.bfloat16)
    return jnp.einsum(
        "th,hd->td", applied, fast[2], preferred_element_type=jnp.float32
    ).astype(jnp.bfloat16)


def section_chain(key_rows, value_rows, query_rows, step_rates, states_in, init_weights):
    tok_count = lax.axis_size("tok")
    feature_width = init_weights.shape[-1]
    part_cols = feature_width // tok_count
    rate_scale = 1.0 / math.sqrt(key_rows.shape[2] * tok_count * feature_width)
    section_index = lax.axis_index("span")
    tok_index = lax.axis_index("tok")
    init_fast = init_weights[0]
    init_full = init_fast.astype(jnp.float32)
    init_norms = jnp.sqrt(jnp.sum(init_full * init_full, axis=-2) + 1e-06)
    own_norms = lax.dynamic_slice_in_dim(init_norms, tok_index * part_cols, part_cols, 1)
    tick_count = key_rows.shape[0]
    results = []
    weights = states_in[0, 0]
    anchor = jnp.abs(weights[0, 0, 0]) + 1.0
    unit = anchor / anchor
    weights = lax.fori_loop(
        0, lax.axis_index("head") * DELAY_STEPS, lambda step, held: held * unit, weights
    )
    fast = gather_cols(weights.astype(jnp.bfloat16), part_cols)
    arrived = None
    earlier_queries = rotated(query_rows[: tick_count - 1, 0, :, 0], "span", 1)
    for tick_number in range(tick_count):
        if tick_number > 0:
            fast = jnp.where(section_index == 0, init_fast, arrived)
            weights = lax.dynamic_slice_in_dim(fast, tok_index * part_cols, part_cols, 2).astype(
                jnp.float32
            )
        key_block = key_rows[tick_number, 0, :, 0]
        scaled = (
            (step_rates[tick_number, 0, 0] * rate_scale)[:, None]
            * value_rows[tick_number, 0, :, 0].astype(jnp.float32)
        ).astype(jnp.bfloat16)
        for update_step in range(ITERS):
            if update_step > 0:
                fast = gather_cols(weights.astype(jnp.bfloat16), part_cols)
            partial = fast_grads(fast, key_block, scaled)
            summed = scatter_sum(partial, part_cols)
            weights = renormalize(weights + summed, own_norms)
        own = weights.astype(jnp.bfloat16)
        if tick_number + 1 < tick_count:
            arrived = cross_gather(own, part_cols)
            for_previous = apply_fast(arrived, earlier_queries[tick_number])
            results.append(rotated(for_previous, "span", -1))
        else:
            fast = gather_cols(own, part_cols)
            results.append(apply_fast(fast, query_rows[tick_number, 0, :, 0]))
    outputs = jnp.stack(results)[:, None, :, None]
    return (outputs, weights[None, None])


def solution(mesh):
    placed = (
        P("groups", "span", "tok", "head", None),
        P("groups", "span", "tok", "head", None),
        P("groups", "span", "tok", "head", None),
        P("groups", "span", "head", "tok"),
        P(("groups", "span"), "head", None, None, "tok"),
        P("head", None, None, None),
    )
    return jax.shard_map(
        section_chain,
        mesh=mesh,
        in_specs=placed,
        out_specs=(
            P("groups", "span", "tok", "head", None),
            P(("groups", "span"), "head", None, None, "tok"),
        ),
        check_vma=False,
    )
```

```python
import math

import jax
import jax.numpy as jnp
from jax import lax
from jax.sharding import PartitionSpec as P


ITERS = 2
DELAY_STEPS = 60


def rotated(value, axis, by):
    devices = lax.axis_size(axis)
    return lax.ppermute(value, axis, [(i, (i + by) % devices) for i in range(devices)])


def scatter_sum(partial, part_cols):
    tok_count = lax.axis_size("tok")
    me = lax.axis_index("tok")
    got = {}
    for by in reversed(range(1, tok_count)):
        chunk = lax.dynamic_slice_in_dim(partial, ((me + by) % tok_count) * part_cols, part_cols, 2)
        got[by] = rotated(chunk, "tok", by)
    total = lax.dynamic_slice_in_dim(partial, me * part_cols, part_cols, 2).astype(jnp.float32)
    for by in range(1, tok_count):
        total = total + got[by].astype(jnp.float32)
    return total


def gather_cols(own, part_cols):
    tok_count = lax.axis_size("tok")
    me = lax.axis_index("tok")
    full = jnp.zeros(own.shape[:2] + (part_cols * tok_count,), own.dtype)
    full = lax.dynamic_update_slice_in_dim(full, own, me * part_cols, 2)
    for by in reversed(range(1, tok_count)):
        got = rotated(own, "tok", by)
        full = lax.dynamic_update_slice_in_dim(full, got, ((me - by) % tok_count) * part_cols, 2)
    return full


def cross_gather(own, part_cols):
    tok_count = lax.axis_size("tok")
    sections = lax.axis_size("span")
    me = lax.axis_index("tok")
    full = jnp.zeros(own.shape[:2] + (part_cols * tok_count,), own.dtype)
    for by in range(tok_count):
        pairs = [
            (t * sections + s, ((t + by) % tok_count) * sections + (s + 1) % sections)
            for t in range(tok_count)
            for s in range(sections)
        ]
        got = lax.ppermute(own, ("tok", "span"), pairs)
        full = lax.dynamic_update_slice_in_dim(full, got, ((me - by) % tok_count) * part_cols, 2)
    return full


def renormalize(matrices, init_norms):
    column_norms = jnp.sqrt(jnp.sum(matrices * matrices, axis=-2) + 1e-06)
    return matrices * (init_norms / column_norms)[..., None, :]


def fast_grads(fast, key_block, scaled):
    gate_pre = jnp.einsum("td,dh->th", key_block, fast[0], preferred_element_type=jnp.float32)
    up_pre = jnp.einsum("td,dh->th", key_block, fast[1], preferred_element_type=jnp.float32)
    sigmoid_gate = jax.nn.sigmoid(gate_pre)
    gated = gate_pre * sigmoid_gate
    hidden = (gated * up_pre).astype(jnp.bfloat16)
    back_grad = jnp.einsum("td,hd->th", scaled, fast[2], preferred_element_type=jnp.float32)
    grad_gate = (
        back_grad * up_pre * sigmoid_gate * (1.0 + gate_pre * (1.0 - sigmoid_gate))
    ).astype(jnp.bfloat16)
    grad_up = (back_grad * gated).astype(jnp.bfloat16)
    first = jnp.einsum("td,th->dh", key_block, grad_gate, preferred_element_type=jnp.float32)
    second = jnp.einsum("td,th->dh", key_block, grad_up, preferred_element_type=jnp.float32)
    third = jnp.einsum("th,td->hd", hidden, scaled, preferred_element_type=jnp.float32)
    return jnp.stack([first, second, third], axis=0).astype(jnp.bfloat16)


def apply_fast(fast, query_block):
    query_gate = jnp.einsum("td,dh->th", query_block, fast[0], preferred_element_type=jnp.float32)
    query_up = jnp.einsum("td,dh->th", query_block, fast[1], preferred_element_type=jnp.float32)
    applied = (query_gate * jax.nn.sigmoid(query_gate) * query_up).astype(jnp.bfloat16)
    return jnp.einsum(
        "th,hd->td", applied, fast[2], preferred_element_type=jnp.float32
    ).astype(jnp.bfloat16)


def section_chain(key_rows, value_rows, query_rows, step_rates, states_in, init_weights):
    tok_count = lax.axis_size("tok")
    feature_width = init_weights.shape[-1]
    part_cols = feature_width // tok_count
    rate_scale = 1.0 / math.sqrt(key_rows.shape[2] * tok_count * feature_width)
    section_index = lax.axis_index("span")
    tok_index = lax.axis_index("tok")
    init_fast = init_weights[0]
    init_full = init_fast.astype(jnp.float32)
    init_norms = jnp.sqrt(jnp.sum(init_full * init_full, axis=-2) + 1e-06)
    own_norms = lax.dynamic_slice_in_dim(init_norms, tok_index * part_cols, part_cols, 1)
    tick_count = key_rows.shape[0]
    results = []
    weights = states_in[0, 0]
    unit = (init_norms[0, 0] + 1.0) / (init_norms[0, 0] + 1.0)
    weights = lax.fori_loop(
        0, lax.axis_index("head") * DELAY_STEPS, lambda step, held: held * unit, weights
    )
    fast = gather_cols(weights.astype(jnp.bfloat16), part_cols)
    arrived = None
    earlier_queries = rotated(query_rows[: tick_count - 1, 0, :, 0], "span", 1)
    for tick_number in range(tick_count):
        if tick_number > 0:
            fast = jnp.where(section_index == 0, init_fast, arrived)
            weights = lax.dynamic_slice_in_dim(fast, tok_index * part_cols, part_cols, 2).astype(
                jnp.float32
            )
        key_block = key_rows[tick_number, 0, :, 0]
        scaled = (
            (step_rates[tick_number, 0, 0] * rate_scale)[:, None]
            * value_rows[tick_number, 0, :, 0].astype(jnp.float32)
        ).astype(jnp.bfloat16)
        for update_step in range(ITERS):
            if update_step > 0:
                fast = gather_cols(weights.astype(jnp.bfloat16), part_cols)
            partial = fast_grads(fast, key_block, scaled)
            summed = scatter_sum(partial, part_cols)
            weights = renormalize(weights + summed, own_norms)
        own = weights.astype(jnp.bfloat16)
        if tick_number + 1 < tick_count:
            arrived = cross_gather(own, part_cols)
            for_previous = apply_fast(arrived, earlier_queries[tick_number])
            results.append(rotated(for_previous, "span", -1))
        else:
            fast = gather_cols(own, part_cols)
            results.append(apply_fast(fast, query_rows[tick_number, 0, :, 0]))
    outputs = jnp.stack(results)[:, None, :, None]
    return (outputs, weights[None, None])


def solution(mesh):
    placed = (
        P("groups", "span", "tok", "head", None),
        P("groups", "span", "tok", "head", None),
        P("groups", "span", "tok", "head", None),
        P("groups", "span", "head", "tok"),
        P(("groups", "span"), "head", None, None, "tok"),
        P("head", None, None, None),
    )
    return jax.shard_map(
        section_chain,
        mesh=mesh,
        in_specs=placed,
        out_specs=(
            P("groups", "span", "tok", "head", None),
            P(("groups", "span"), "head", None, None, "tok"),
        ),
        check_vma=False,
    )
```

```python
import math

import jax
import jax.numpy as jnp
from jax import lax
from jax.sharding import PartitionSpec as P


ITERS = 2
DELAY_STEPS = 80


def rotated(value, axis, by):
    devices = lax.axis_size(axis)
    return lax.ppermute(value, axis, [(i, (i + by) % devices) for i in range(devices)])


def scatter_sum(partial, part_cols):
    tok_count = lax.axis_size("tok")
    me = lax.axis_index("tok")
    total = lax.dynamic_slice_in_dim(partial, me * part_cols, part_cols, 2).astype(jnp.float32)
    for by in range(1, tok_count):
        chunk = lax.dynamic_slice_in_dim(partial, ((me + by) % tok_count) * part_cols, part_cols, 2)
        total = total + rotated(chunk, "tok", by).astype(jnp.float32)
    return total


def gather_cols(own, part_cols):
    tok_count = lax.axis_size("tok")
    me = lax.axis_index("tok")
    full = jnp.zeros(own.shape[:2] + (part_cols * tok_count,), own.dtype)
    full = lax.dynamic_update_slice_in_dim(full, own, me * part_cols, 2)
    for by in range(1, tok_count):
        got = rotated(own, "tok", by)
        full = lax.dynamic_update_slice_in_dim(full, got, ((me - by) % tok_count) * part_cols, 2)
    return full


def cross_gather(own, part_cols):
    tok_count = lax.axis_size("tok")
    sections = lax.axis_size("span")
    me = lax.axis_index("tok")
    full = jnp.zeros(own.shape[:2] + (part_cols * tok_count,), own.dtype)
    for by in range(tok_count):
        pairs = [
            (t * sections + s, ((t + by) % tok_count) * sections + (s + 1) % sections)
            for t in range(tok_count)
            for s in range(sections)
        ]
        got = lax.ppermute(own, ("tok", "span"), pairs)
        full = lax.dynamic_update_slice_in_dim(full, got, ((me - by) % tok_count) * part_cols, 2)
    return full


def renormalize(matrices, init_norms):
    column_norms = jnp.sqrt(jnp.sum(matrices * matrices, axis=-2) + 1e-06)
    return matrices * (init_norms / column_norms)[..., None, :]


def fast_grads(fast, key_block, scaled):
    gate_pre = jnp.einsum("td,dh->th", key_block, fast[0], preferred_element_type=jnp.float32)
    up_pre = jnp.einsum("td,dh->th", key_block, fast[1], preferred_element_type=jnp.float32)
    sigmoid_gate = jax.nn.sigmoid(gate_pre)
    gated = gate_pre * sigmoid_gate
    hidden = (gated * up_pre).astype(jnp.bfloat16)
    back_grad = jnp.einsum("td,hd->th", scaled, fast[2], preferred_element_type=jnp.float32)
    grad_gate = (
        back_grad * up_pre * sigmoid_gate * (1.0 + gate_pre * (1.0 - sigmoid_gate))
    ).astype(jnp.bfloat16)
    grad_up = (back_grad * gated).astype(jnp.bfloat16)
    first = jnp.einsum("td,th->dh", key_block, grad_gate, preferred_element_type=jnp.float32)
    second = jnp.einsum("td,th->dh", key_block, grad_up, preferred_element_type=jnp.float32)
    third = jnp.einsum("th,td->hd", hidden, scaled, preferred_element_type=jnp.float32)
    return jnp.stack([first, second, third], axis=0).astype(jnp.bfloat16)


def apply_fast(fast, query_block):
    query_gate = jnp.einsum("td,dh->th", query_block, fast[0], preferred_element_type=jnp.float32)
    query_up = jnp.einsum("td,dh->th", query_block, fast[1], preferred_element_type=jnp.float32)
    applied = (query_gate * jax.nn.sigmoid(query_gate) * query_up).astype(jnp.bfloat16)
    return jnp.einsum(
        "th,hd->td", applied, fast[2], preferred_element_type=jnp.float32
    ).astype(jnp.bfloat16)


def section_chain(key_rows, value_rows, query_rows, step_rates, states_in, init_weights):
    tok_count = lax.axis_size("tok")
    feature_width = init_weights.shape[-1]
    part_cols = feature_width // tok_count
    rate_scale = 1.0 / math.sqrt(key_rows.shape[2] * tok_count * feature_width)
    section_index = lax.axis_index("span")
    tok_index = lax.axis_index("tok")
    init_fast = init_weights[0]
    init_full = init_fast.astype(jnp.float32)
    init_norms = jnp.sqrt(jnp.sum(init_full * init_full, axis=-2) + 1e-06)
    own_norms = lax.dynamic_slice_in_dim(init_norms, tok_index * part_cols, part_cols, 1)
    tick_count = key_rows.shape[0]
    results = []
    weights = states_in[0, 0]
    unit = (init_norms[0, 0] + 1.0) / (init_norms[0, 0] + 1.0)
    weights = lax.fori_loop(
        0, lax.axis_index("head") * DELAY_STEPS, lambda step, held: held * unit, weights
    )
    fast = gather_cols(weights.astype(jnp.bfloat16), part_cols)
    arrived = None
    earlier_queries = rotated(query_rows[: tick_count - 1, 0, :, 0], "span", 1)
    for tick_number in range(tick_count):
        if tick_number > 0:
            fast = jnp.where(section_index == 0, init_fast, arrived)
            weights = lax.dynamic_slice_in_dim(fast, tok_index * part_cols, part_cols, 2).astype(
                jnp.float32
            )
        key_block = key_rows[tick_number, 0, :, 0]
        scaled = (
            (step_rates[tick_number, 0, 0] * rate_scale)[:, None]
            * value_rows[tick_number, 0, :, 0].astype(jnp.float32)
        ).astype(jnp.bfloat16)
        for update_step in range(ITERS):
            if update_step > 0:
                fast = gather_cols(weights.astype(jnp.bfloat16), part_cols)
            partial = fast_grads(fast, key_block, scaled)
            summed = scatter_sum(partial, part_cols)
            weights = renormalize(weights + summed, own_norms)
        own = weights.astype(jnp.bfloat16)
        if tick_number + 1 < tick_count:
            arrived = cross_gather(own, part_cols)
            for_previous = apply_fast(arrived, earlier_queries[tick_number])
            results.append(rotated(for_previous, "span", -1))
        else:
            fast = gather_cols(own, part_cols)
            results.append(apply_fast(fast, query_rows[tick_number, 0, :, 0]))
    outputs = jnp.stack(results)[:, None, :, None]
    return (outputs, weights[None, None])


def solution(mesh):
    placed = (
        P("groups", "span", "tok", "head", None),
        P("groups", "span", "tok", "head", None),
        P("groups", "span", "tok", "head", None),
        P("groups", "span", "head", "tok"),
        P(("groups", "span"), "head", None, None, "tok"),
        P("head", None, None, None),
    )
    return jax.shard_map(
        section_chain,
        mesh=mesh,
        in_specs=placed,
        out_specs=(
            P("groups", "span", "tok", "head", None),
            P(("groups", "span"), "head", None, None, "tok"),
        ),
        check_vma=False,
    )
```
